256 devices in a mesh: sec: 2 (over core), gx: 16 (over y, x), gy: 8 (over z).
Axes of the slice: x: 4, y: 4, z: 8, core: 2. Of those that a mesh axis runs over, the one named last changes fastest.
Arguments:
- adjoint_state: float32 [2, 10, 2048, 1024], P('sec', None, 'gx', 'gy'), may hold values from -6 to 6
- forcing: float32 [2, 10, 2048, 1024], P('sec', None, 'gx', 'gy'), may hold values from -6 to 6
- viscosity: float32 [2, 2048, 1024], P('sec', 'gx', 'gy'), may hold values from 0.5 to 4
- reaction: float32 [2, 2048, 1024], P('sec', 'gx', 'gy'), may hold values from 0.1 to 1
- source_patch: int32 [2, 16384], P('sec', ('gx', 'gy')), may hold values from 0 to 63
- owner: int32 [2, 16384, 1], P('sec', ('gx', 'gy')), may hold values from 0 to 127; in each aligned block of 128 rows (0 to 127, 128 to 255, ..., all dimensions but the last counted through in order) at most 2 rows name the same one
- cavity_map: int32 [2, 128, 128, 2], P('sec', ('gx', 'gy')), may hold values from 0 to 63
Outputs:
- adjoint_field: float32 [2, 10, 2048, 1024], P('sec', None, 'gx', 'gy')
The draws below stay inside these ranges and needn't reach their ends.
Inputs may be any that keep to these rules, and one draw needn't show every extreme that they name: The entries of one device name each owner at most 2 times, a bound that some block reaches.
All inputs are finite; a program needn't handle non-finite values.
Results may differ from the reference program's by a relative error of at most 0.00002.
Values sent between devices are 32-bit elements; how exact they have to be, the bound alone decides.
No kernel may reach another device: no remote copies, remote signals or barrier semaphores. Data moves between devices by JAX's collectives and lax.ppermute only.
A program may use at most 64 MiB of HBM per device.

```python
import math
import jax
import jax.numpy as jnp
import numpy as np

LEV = 10
CX = 128
CY = 128
PATCH = 2
PW = 128
SWEEPS = 8
TPD = 128
GRID_DEV = 128
CAP = 2
NPATCH = 64
NX = 2048
NY = 1024
N_GX = 16
N_GY = 8


def place_ends(values, key, low, high):
    dims = values.shape
    spot = [jax.random.randint(jax.random.fold_in(key, axis), (), 0, dims[axis]) for axis in range(len(dims))]
    values = values.at[tuple(spot)].set(low)
    longest = dims.index(max(dims))
    spot[longest] = (spot[longest] + 1) % dims[longest]
    return values.at[tuple(spot)].set(high)


def level_of(rng, dims, cuts, low, top_value):
    level = 1.0
    for dim, shards_of in cuts:
        steps = jax.random.uniform(jax.random.fold_in(jax.random.fold_in(rng, 6), dim), (shards_of,), jnp.float32, low / len(cuts), top_value / len(cuts))
        level = level * jnp.repeat(jnp.exp(steps), dims[dim] // shards_of).reshape((-1,) + (1,) * (len(dims) - 1 - dim))
    return level


def assign_block(rng, own, number, rows, number_of, top, reach, skew):
    ranking = jax.random.permutation(rng, number_of)
    packed, usual = load_shares(number_of, rows * top, reach, skew, True), load_shares(number_of, rows * top, reach, skew, False)
    places = jnp.arange(number_of)

    def named(lengths, rotation):
        used = int((lengths > 0).sum())
        fixed = max(1, used // 4)
        passed = fixed + (places - fixed + rotation * (used - fixed)) % max(1, number_of - fixed)
        return jnp.zeros((number_of,), jnp.int32).at[ranking[jnp.where(places < fixed, places, passed)]].set(jnp.asarray(lengths, jnp.int32))

    lengths = jnp.where(number % 4 == 0, named(packed, number // 4), named(usual, number - number // 4 - 1))
    mixed = jax.random.permutation(jax.random.fold_in(own, 3), number_of)
    giver, taker = mixed[0:number_of // 2 * 2:2], mixed[1:number_of // 2 * 2:2]
    room = jnp.minimum(lengths[giver] - 1, reach - lengths[taker]) // 2
    room = jnp.where((giver == ranking[0]) | (taker == ranking[0]) | (lengths[taker] == 0), 0, jnp.maximum(room, 0))
    passed = jax.random.randint(jax.random.fold_in(own, 4), (number_of // 2,), 0, 1 << 20) % (room + 1)
    lengths = lengths.at[giver].add(-passed).at[taker].add(passed)
    items = jnp.searchsorted(jnp.cumsum(lengths), jnp.arange(rows * top), side="right").astype(jnp.int32)
    table = items.reshape(top, rows).T
    table = table[jax.random.permutation(jax.random.fold_in(own, 1), rows)]
    rotation = jax.random.randint(jax.random.fold_in(own, 2), (rows, 1), 0, top)
    return jnp.take_along_axis(table, (jnp.arange(top)[None, :] + rotation) % top, axis=1)


def load_shares(count, total, most, skew, full):
    loads = [(1 << 20) // math.isqrt(rank ** skew) + 1 for rank in range(1, count + 1)]
    largest = most if full else min(most, max(-(-total // count), total * loads[0] // sum(loads)))
    least = 1 if total - largest >= count - 1 else 0
    counts, rest = [largest] + [least] * (count - 1), total - largest - least * (count - 1)
    while rest > 0:
        free = [i for i in range(1, count) if counts[i] < largest] or [i for i in range(1, count) if counts[i] < most]
        mass, budget = sum([loads[i] for i in free]), rest
        for i in free:
            more = min(most - counts[i], max(1, budget * loads[i] // mass), rest)
            counts[i] = counts[i] + more
            rest = rest - more
    return np.array(counts)


def noise(rng, dims, scale, most, cuts=(), held_as=jnp.bfloat16):
    array = scale * jax.random.normal(rng, dims, jnp.float32)
    if cuts:
        array = array * level_of(rng, dims, cuts, -0.22, 0.18)
    return jnp.clip(array, -most, most).astype(held_as)


def setup_inputs(seed: int = 0) -> dict:
    seeds = jax.random.split(jax.random.key(seed), 8)
    adjoint_state = noise(seeds[0], (2, LEV, NX, NY), 1.0, 6.0, ((0, 2), (2, 16), (3, 8)), jnp.float32)
    forcing = noise(seeds[1], (2, LEV, NX, NY), 1.0, 6.0, ((0, 2), (2, 16), (3, 8)), jnp.float32)
    viscosity = jnp.clip(jnp.exp(math.log(4.0) - 2.0794415 * jax.random.uniform(seeds[2], (2, NX, NY), jnp.float32) ** level_of(seeds[2], (2, NX, NY), ((0, 2), (1, 16), (2, 8)), -0.2, 0.2)), 0.5, 4.0)
    reaction = jnp.clip(jnp.exp(math.log(1.0) - 2.3025851 * jax.random.uniform(seeds[3], (2, NX, NY), jnp.float32) ** level_of(seeds[3], (2, NX, NY), ((0, 2), (1, 16), (2, 8)), -0.2, 0.2)), 0.1, 1.0)
    source_patch = place_ends(jax.random.randint(seeds[4], (2, GRID_DEV * TPD), 0, NPATCH), jax.random.fold_in(seeds[4], 1), 0, NPATCH - 1).astype(jnp.int32)
    owner_keys = jax.random.split(jax.random.fold_in(seeds[5], 1), 2 * (GRID_DEV * TPD) // TPD)
    owner_turns = jax.random.permutation(jax.random.fold_in(seeds[5], 3), 2 * (GRID_DEV * TPD) // TPD)
    owner = jax.vmap(lambda own, number: assign_block(jax.random.fold_in(seeds[5], 2), own, number, TPD, GRID_DEV, 1, CAP, 2))(owner_keys, owner_turns).reshape((2, GRID_DEV * TPD, 1))
    cavity_map = place_ends(jax.random.randint(seeds[6], (2, GRID_DEV, GRID_DEV, CAP), 0, NPATCH), jax.random.fold_in(seeds[6], 1), 0, NPATCH - 1).astype(jnp.int32)
    return {"adjoint_state": adjoint_state, "forcing": forcing, "viscosity": viscosity, "reaction": reaction, "source_patch": source_patch, "owner": owner, "cavity_map": cavity_map}


OMEGA = 0.8
KAPPA = 0.5


def relax_all(field, visc, invd, force):
    padded = jnp.pad(field, ((0, 0), (0, 0), (1, 1), (1, 1)))
    beside = padded[:, :, 2:, 1:-1] + padded[:, :, :-2, 1:-1]
    beside = beside + padded[:, :, 1:-1, 2:] + padded[:, :, 1:-1, :-2]
    return (1.0 - OMEGA) * field + OMEGA * invd * (force + visc * beside)


def reference(adjoint_state, forcing, viscosity, reaction, source_patch, owner, cavity_map):
    groups = N_GX * N_GY
    invd = (1.0 / (4.0 * viscosity + reaction))[:, None]
    visc = viscosity[:, None]
    field = adjoint_state
    for step in range(SWEEPS // 2):
        field = relax_all(field, visc, invd, forcing)
    blocks = field.reshape(2, LEV, N_GX, CX // PATCH, PATCH, N_GY, CY // PW, PW)
    patches = blocks.transpose(0, 2, 5, 3, 6, 1, 4, 7).reshape(2, groups, NPATCH, LEV, PATCH, PW)
    srcs = source_patch.reshape(2, groups, TPD)
    dests = owner.reshape(2, groups, TPD)
    sidx = jnp.broadcast_to(jnp.arange(2, dtype=jnp.int32)[:, None, None], srcs.shape)
    gidx = jnp.broadcast_to(jnp.arange(groups, dtype=jnp.int32)[None, :, None], srcs.shape)
    oidx = 1 - sidx
    onehot = (dests[..., None] == jnp.arange(groups, dtype=jnp.int32)).astype(jnp.int32)
    before = jnp.cumsum(onehot, axis=2) - onehot
    rank = jnp.sum(before * onehot, axis=3).astype(jnp.int32)
    recv = cavity_map[oidx, dests, gidx, rank]
    sent = patches[sidx, gidx, srcs]
    local = patches[oidx, dests, recv]
    updated = patches.at[oidx, dests, recv].add(KAPPA * sent)
    updated = updated.at[sidx, gidx, srcs].add(local * jnp.tanh(sent))
    blocks = updated.reshape(2, N_GX, N_GY, CX // PATCH, CY // PW, LEV, PATCH, PW)
    field = blocks.transpose(0, 5, 1, 3, 6, 2, 4, 7).reshape(2, LEV, N_GX * CX, N_GY * CY)
    for step in range(SWEEPS // 2):
        field = relax_all(field, visc, invd, forcing)
    return field
```

```python
import jax
import jax.numpy as jnp
from jax import lax
from jax.sharding import PartitionSpec as P

PATCH = 2
PW = 128
SWEEPS = 8


OMEGA = 0.8
KAPPA = 0.5
HIGHEST = lax.Precision.HIGHEST


def shifted(block, dx, dy):
    nx = lax.axis_size("gx")
    ny = lax.axis_size("gy")
    pairs = []
    for a in range(nx):
        for b in range(ny):
            sa, sb = a + dx, b + dy
            if 0 <= sa < nx and 0 <= sb < ny:
                pairs.append((sa * ny + sb, a * ny + b))
    return lax.ppermute(block, ("gx", "gy"), pairs)


def halo(cells, w):
    top, bot = cells[:, :w], cells[:, -w:]
    left, right = cells[:, :, :w], cells[:, :, -w:]
    north = shifted(bot, -1, 0)
    south = shifted(top, 1, 0)
    west = shifted(right, 0, -1)
    east = shifted(left, 0, 1)
    nw = shifted(cells[:, -w:, -w:], -1, -1)
    ne = shifted(cells[:, -w:, :w], -1, 1)
    sw = shifted(cells[:, :w, -w:], 1, -1)
    se = shifted(cells[:, :w, :w], 1, 1)
    rows = [
        jnp.concatenate([nw, north, ne], axis=2),
        jnp.concatenate([west, cells, east], axis=2),
        jnp.concatenate([sw, south, se], axis=2),
    ]
    return jnp.concatenate(rows, axis=1)


def relax(field, visc, invd, force):
    padded = jnp.pad(field, ((0, 0), (1, 1), (1, 1)))
    beside = padded[:, 2:, 1:-1] + padded[:, :-2, 1:-1]
    beside = beside + padded[:, 1:-1, 2:] + padded[:, 1:-1, :-2]
    return (1.0 - OMEGA) * field + OMEGA * invd * (force + visc * beside)


def sweeps(ext, visc, invd, force, count, w):
    for _ in range(count):
        ext = relax(ext, visc, invd, force)
    return ext[:, w:-w, w:-w]


def swap_sec(x):
    return lax.ppermute(x, "sec", [(0, 1), (1, 0)])


def onehot(index, size):
    return (index[:, None] == jnp.arange(size, dtype=jnp.int32)[None, :]).astype(jnp.float32)


def pick(sel, patches):
    return jnp.einsum("jk,lkrc->jlrc", sel, patches, precision=HIGHEST)


def spread(sel, values):
    return jnp.einsum("jk,jlrc->lkrc", sel, values, precision=HIGHEST)


def couple(x1, source_patch, owner, cavity_map):
    levels, rows, cols = x1.shape
    npatch = rows // PATCH
    groups, slots_per = cavity_map.shape[2], cavity_map.shape[3]
    nslot = groups * slots_per
    mine = x1.reshape(levels, npatch, PATCH, cols)
    other = swap_sec(mine)
    sources = source_patch[0]
    dest = owner[0, :, 0]
    count = dest.shape[0]
    earlier = jnp.arange(count)[None, :] < jnp.arange(count)[:, None]
    rank = jnp.sum((dest[:, None] == dest[None, :]) & earlier, axis=1).astype(jnp.int32)
    slot = dest * slots_per + rank
    send_sel = jnp.dot(onehot(slot, nslot).T, onehot(sources, npatch), precision=HIGHEST)
    cav_other = swap_sec(cavity_map[0, 0].reshape(-1))
    recv_sel = onehot(cav_other, npatch)
    sent = pick(send_sel, mine)
    local = pick(recv_sel, other)
    chunk = (groups, slots_per * levels * PATCH, cols)
    outgoing = jnp.concatenate([sent.reshape(chunk), local.reshape(chunk)], axis=1)
    incoming = lax.all_to_all(outgoing, ("gx", "gy"), 0, 0, tiled=True)
    half = slots_per * levels * PATCH
    arrived = incoming[:, :half].reshape(nslot, levels, PATCH, cols)
    answer = incoming[:, half:].reshape(nslot, levels, PATCH, cols)
    for_other = spread(recv_sel, KAPPA * arrived)
    for_mine = spread(send_sel, answer * jnp.tanh(sent))
    updated = mine + swap_sec(for_other) + for_mine
    return updated.reshape(levels, rows, cols)


def body(adjoint_state, forcing, viscosity, reaction, source_patch, owner, cavity_map):
    w = SWEEPS // 2
    levels = adjoint_state.shape[1]
    invd = 1.0 / (4.0 * viscosity + reaction)
    stacked = jnp.concatenate([adjoint_state[0], forcing[0], viscosity, invd], axis=0)
    ext = halo(stacked, w)
    field = ext[:levels]
    force = ext[levels:2 * levels]
    visc = ext[2 * levels:2 * levels + 1]
    inv_wide = ext[2 * levels + 1:]
    x1 = sweeps(field, visc, inv_wide, force, w, w)
    x2 = couple(x1, source_patch, owner, cavity_map)
    out = sweeps(halo(x2, w), visc, inv_wide, force, SWEEPS - w, w)
    return out[None]


def solution(mesh):
    return jax.shard_map(
        body,
        mesh=mesh,
        in_specs=(
            P("sec", None, "gx", "gy"),
            P("sec", None, "gx", "gy"),
            P("sec", "gx", "gy"),
            P("sec", "gx", "gy"),
            P("sec", ("gx", "gy")),
            P("sec", ("gx", "gy"), None),
            P("sec", ("gx", "gy"), None, None),
        ),
        out_specs=P("sec", None, "gx", "gy"),
        check_vma=False,
    )
```

```python
import jax
import jax.numpy as jnp
from jax import lax
from jax.sharding import PartitionSpec as P

PATCH = 2
PW = 128
SWEEPS = 8


OMEGA = 0.8
KAPPA = 0.5
HIGHEST = lax.Precision.HIGHEST


def shifted(block, dx, dy):
    nx = lax.axis_size("gx")
    ny = lax.axis_size("gy")
    pairs = []
    for a in range(nx):
        for b in range(ny):
            sa, sb = a + dx, b + dy
            if 0 <= sa < nx and 0 <= sb < ny:
                pairs.append((sa * ny + sb, a * ny + b))
    return lax.ppermute(block, ("gx", "gy"), pairs)


def halo(cells, w):
    west = shifted(cells[:, :, -w:], 0, -1)
    east = shifted(cells[:, :, :w], 0, 1)
    wide = jnp.concatenate([west, cells, east], axis=2)
    north = shifted(wide[:, -w:], -1, 0)
    south = shifted(wide[:, :w], 1, 0)
    return jnp.concatenate([north, wide, south], axis=1)


def relax(field, visc, invd, force):
    padded = jnp.pad(field, ((0, 0), (1, 1), (1, 1)))
    beside = padded[:, 2:, 1:-1] + padded[:, :-2, 1:-1]
    beside = beside + padded[:, 1:-1, 2:] + padded[:, 1:-1, :-2]
    return (1.0 - OMEGA) * field + OMEGA * invd * (force + visc * beside)


def sweeps(ext, visc, invd, force, count, w):
    for _ in range(count):
        ext = relax(ext, visc, invd, force)
    return ext[:, w:-w, w:-w]


def swap_sec(x):
    return lax.ppermute(x, "sec", [(0, 1), (1, 0)])


def onehot(index, size):
    return (index[:, None] == jnp.arange(size, dtype=jnp.int32)[None, :]).astype(jnp.float32)


def mm(a, b):
    return jnp.dot(a, b, precision=HIGHEST)


def selectors(source_patch, owner, cavity_map, npatch):
    groups, slots_per = cavity_map.shape[2], cavity_map.shape[3]
    sources = source_patch[0]
    dest = owner[0, :, 0]
    count = dest.shape[0]
    earlier = jnp.arange(count)[None, :] < jnp.arange(count)[:, None]
    rank = jnp.sum((dest[:, None] == dest[None, :]) & earlier, axis=1).astype(jnp.int32)
    by_owner = onehot(dest, groups)
    by_source = onehot(sources, npatch)
    send = [mm((by_owner * (rank == r).astype(jnp.float32)[:, None]).T, by_source) for r in range(slots_per)]
    cav_other = swap_sec(cavity_map[0, 0])
    recv = [onehot(cav_other[:, r], npatch) for r in range(slots_per)]
    return send, recv


def couple(x1, sel):
    send, recv = sel
    levels, rows, cols = x1.shape
    npatch = rows // PATCH
    width = levels * PATCH * cols
    mine = x1.reshape(levels, npatch, PATCH * cols).transpose(1, 0, 2).reshape(npatch, width)
    other = swap_sec(mine)
    sent = [mm(g, mine) for g in send]
    local = [mm(g, other) for g in recv]
    outgoing = jnp.concatenate(sent + local, axis=1)
    incoming = lax.all_to_all(outgoing, ("gx", "gy"), 0, 0, tiled=True)
    nr = len(send)
    arrived = [incoming[:, r * width:(r + 1) * width] for r in range(nr)]
    answer = [incoming[:, (nr + r) * width:(nr + r + 1) * width] for r in range(nr)]
    for_other = mm(recv[0].T, KAPPA * arrived[0])
    for_mine = mm(send[0].T, answer[0] * jnp.tanh(sent[0]))
    for r in range(1, nr):
        for_other = for_other + mm(recv[r].T, KAPPA * arrived[r])
        for_mine = for_mine + mm(send[r].T, answer[r] * jnp.tanh(sent[r]))
    updated = mine + swap_sec(for_other) + for_mine
    return updated.reshape(npatch, levels, PATCH * cols).transpose(1, 0, 2).reshape(levels, rows, cols)


def body(adjoint_state, forcing, viscosity, reaction, source_patch, owner, cavity_map):
    w = SWEEPS // 2
    levels, rows, cols = adjoint_state.shape[1:]
    invd = 1.0 / (4.0 * viscosity + reaction)
    stacked = jnp.concatenate([adjoint_state[0], forcing[0], viscosity, invd], axis=0)
    ext = halo(stacked, w)
    field = ext[:levels]
    force = ext[levels:2 * levels]
    visc = ext[2 * levels:2 * levels + 1]
    inv_wide = ext[2 * levels + 1:]
    sel = selectors(source_patch, owner, cavity_map, rows // PATCH)
    x1 = sweeps(field, visc, inv_wide, force, w, w)
    x2 = couple(x1, sel)
    out = sweeps(halo(x2, w), visc, inv_wide, force, SWEEPS - w, w)
    return out[None]


def solution(mesh):
    return jax.shard_map(
        body,
        mesh=mesh,
        in_specs=(
            P("sec", None, "gx", "gy"),
            P("sec", None, "gx", "gy"),
            P("sec", "gx", "gy"),
            P("sec", "gx", "gy"),
            P("sec", ("gx", "gy")),
            P("sec", ("gx", "gy"), None),
            P("sec", ("gx", "gy"), None, None),
        ),
        out_specs=P("sec", None, "gx", "gy"),
        check_vma=False,
    )
```

```python
import jax
import jax.numpy as jnp
from jax import lax
from jax.sharding import PartitionSpec as P

PATCH = 2
PW = 128
SWEEPS = 8


OMEGA = 0.8
KAPPA = 0.5
HIGHEST = lax.Precision.HIGHEST


def shifted(block, dx, dy):
    nx = lax.axis_size("gx")
    ny = lax.axis_size("gy")
    pairs = []
    for a in range(nx):
        for b in range(ny):
            sa, sb = a + dx, b + dy
            if 0 <= sa < nx and 0 <= sb < ny:
                pairs.append((sa * ny + sb, a * ny + b))
    return lax.ppermute(block, ("gx", "gy"), pairs)


def halo(cells, w):
    west = shifted(cells[:, :, -w:], 0, -1)
    east = shifted(cells[:, :, :w], 0, 1)
    wide = jnp.concatenate([west, cells, east], axis=2)
    north = shifted(wide[:, -w:], -1, 0)
    south = shifted(wide[:, :w], 1, 0)
    return jnp.concatenate([north, wide, south], axis=1)


def relax(field, visc, invd, force):
    padded = jnp.pad(field, ((0, 0), (1, 1), (1, 1)))
    beside = padded[:, 2:, 1:-1] + padded[:, :-2, 1:-1]
    beside = beside + padded[:, 1:-1, 2:] + padded[:, 1:-1, :-2]
    return (1.0 - OMEGA) * field + OMEGA * invd * (force + visc * beside)


def sweeps(ext, visc, invd, force, count, w):
    for _ in range(count):
        ext = relax(ext, visc, invd, force)
    return ext[:, w:-w, w:-w]


def swap_sec(x):
    return lax.ppermute(x, "sec", [(0, 1), (1, 0)])


def onehot(index, size):
    return (index[:, None] == jnp.arange(size, dtype=jnp.int32)[None, :]).astype(jnp.float32)


def pick(sel, patches):
    return jnp.einsum("jk,lkrc->jlrc", sel, patches, precision=HIGHEST)


def spread(sel, values):
    return jnp.einsum("jk,jlrc->lkrc", sel, values, precision=HIGHEST)


def selectors(source_patch, owner, cavity_map, npatch):
    groups, slots_per = cavity_map.shape[2], cavity_map.shape[3]
    nslot = groups * slots_per
    sources = source_patch[0]
    dest = owner[0, :, 0]
    count = dest.shape[0]
    earlier = jnp.arange(count)[None, :] < jnp.arange(count)[:, None]
    rank = jnp.sum((dest[:, None] == dest[None, :]) & earlier, axis=1).astype(jnp.int32)
    slot = dest * slots_per + rank
    send_sel = jnp.dot(onehot(slot, nslot).T, onehot(sources, npatch), precision=HIGHEST)
    cav_other = swap_sec(cavity_map[0, 0].reshape(-1))
    recv_sel = onehot(cav_other, npatch)
    return send_sel, recv_sel, groups, slots_per


def couple(x1, sel):
    send_sel, recv_sel, groups, slots_per = sel
    levels, rows, cols = x1.shape
    npatch = rows // PATCH
    nslot = groups * slots_per
    mine = x1.reshape(levels, npatch, PATCH, cols)
    other = swap_sec(mine)
    sent = pick(send_sel, mine)
    local = pick(recv_sel, other)
    half = slots_per * levels * PATCH
    chunk = (groups, half, cols)
    outgoing = jnp.concatenate([sent.reshape(chunk), local.reshape(chunk)], axis=1)
    incoming = lax.all_to_all(outgoing, ("gx", "gy"), 0, 0, tiled=True)
    arrived = incoming[:, :half].reshape(nslot, levels, PATCH, cols)
    answer = incoming[:, half:].reshape(nslot, levels, PATCH, cols)
    for_other = spread(recv_sel, KAPPA * arrived)
    for_mine = spread(send_sel, answer * jnp.tanh(sent))
    updated = mine + swap_sec(for_other) + for_mine
    return updated.reshape(levels, rows, cols)


def body(adjoint_state, forcing, viscosity, reaction, source_patch, owner, cavity_map):
    w = SWEEPS // 2
    levels, rows, cols = adjoint_state.shape[1:]
    invd = 1.0 / (4.0 * viscosity + reaction)
    stacked = jnp.concatenate([adjoint_state[0], forcing[0], viscosity, invd], axis=0)
    ext = halo(stacked, w)
    field = ext[:levels]
    force = ext[levels:2 * levels]
    visc = ext[2 * levels:2 * levels + 1]
    inv_wide = ext[2 * levels + 1:]
    sel = selectors(source_patch, owner, cavity_map, rows // PATCH)
    x1 = sweeps(field, visc, inv_wide, force, w, w)
    x2 = couple(x1, sel)
    out = sweeps(halo(x2, w), visc, inv_wide, force, SWEEPS - w, w)
    return out[None]


def solution(mesh):
    return jax.shard_map(
        body,
        mesh=mesh,
        in_specs=(
            P("sec", None, "gx", "gy"),
            P("sec", None, "gx", "gy"),
            P("sec", "gx", "gy"),
            P("sec", "gx", "gy"),
            P("sec", ("gx", "gy")),
            P("sec", ("gx", "gy"), None),
            P("sec", ("gx", "gy"), None, None),
        ),
        out_specs=P("sec", None, "gx", "gy"),
        check_vma=False,
    )
```

```python
import jax
import jax.numpy as jnp
from jax import lax
from jax.sharding import PartitionSpec as P
from jax.experimental import pallas as pl
from jax.experimental.pallas import tpu as pltpu

PATCH = 2
PW = 128
SWEEPS = 8


OMEGA = 0.8
KAPPA = 0.5
HIGHEST = lax.Precision.HIGHEST


def shifted(block, dx, dy):
    nx = lax.axis_size("gx")
    ny = lax.axis_size("gy")
    pairs = []
    for a in range(nx):
        for b in range(ny):
            sa, sb = a + dx, b + dy
            if 0 <= sa < nx and 0 <= sb < ny:
                pairs.append((sa * ny + sb, a * ny + b))
    return lax.ppermute(block, ("gx", "gy"), pairs)


def halo(cells, w):
    chans, rows, cols = cells.shape
    west = shifted(cells[:, :, -w:], 0, -1)
    east = shifted(cells[:, :, :w], 0, 1)
    gap = jnp.zeros((chans, rows, cols - 2 * w), cells.dtype)
    wide = jnp.concatenate([cells, east, gap, west], axis=2)
    north = shifted(wide[:, -w:], -1, 0)
    south = shifted(wide[:, :w], 1, 0)
    return jnp.concatenate([wide, south, north], axis=1)


def sweeps(ext, visc, invd, force, count, rows, cols):
    levels, height, lanes = ext.shape

    def kernel(x_ref, v_ref, i_ref, f_ref, o_ref):
        v = v_ref[0]
        inv = i_ref[0]

        def level(l, carry):
            x = x_ref[l]
            f = f_ref[l]
            for _ in range(count):
                beside = pltpu.roll(x, 1, 0) + pltpu.roll(x, height - 1, 0)
                beside = beside + pltpu.roll(x, 1, 1) + pltpu.roll(x, lanes - 1, 1)
                x = (1.0 - OMEGA) * x + OMEGA * inv * (f + v * beside)
            o_ref[l] = x[:rows, :cols]
            return carry

        lax.fori_loop(0, levels, level, 0)

    return pl.pallas_call(
        kernel, out_shape=jax.ShapeDtypeStruct((levels, rows, cols), jnp.float32)
    )(ext, visc, invd, force)


def swap_sec(x):
    return lax.ppermute(x, "sec", [(0, 1), (1, 0)])


def onehot(index, size):
    return (index[:, None] == jnp.arange(size, dtype=jnp.int32)[None, :]).astype(jnp.float32)


def pick(sel, patches):
    return jnp.einsum("jk,lkrc->jlrc", sel, patches, precision=HIGHEST)


def spread(sel, values):
    return jnp.einsum("jk,jlrc->lkrc", sel, values, precision=HIGHEST)


def selectors(source_patch, owner, cavity_map, npatch):
    groups, slots_per = cavity_map.shape[2], cavity_map.shape[3]
    nslot = groups * slots_per
    sources = source_patch[0]
    dest = owner[0, :, 0]
    count = dest.shape[0]
    earlier = jnp.arange(count)[None, :] < jnp.arange(count)[:, None]
    rank = jnp.sum((dest[:, None] == dest[None, :]) & earlier, axis=1).astype(jnp.int32)
    slot = dest * slots_per + rank
    send_sel = jnp.dot(onehot(slot, nslot).T, onehot(sources, npatch), precision=HIGHEST)
    cav_other = swap_sec(cavity_map[0, 0].reshape(-1))
    recv_sel = onehot(cav_other, npatch)
    return send_sel, recv_sel, groups, slots_per


def couple(x1, sel):
    send_sel, recv_sel, groups, slots_per = sel
    levels, rows, cols = x1.shape
    npatch = rows // PATCH
    nslot = groups * slots_per
    mine = x1.reshape(levels, npatch, PATCH, cols)
    other = swap_sec(mine)
    sent = pick(send_sel, mine)
    local = pick(recv_sel, other)
    half = slots_per * levels * PATCH
    chunk = (groups, half, cols)
    outgoing = jnp.concatenate([sent.reshape(chunk), local.reshape(chunk)], axis=1)
    incoming = lax.all_to_all(outgoing, ("gx", "gy"), 0, 0, tiled=True)
    arrived = incoming[:, :half].reshape(nslot, levels, PATCH, cols)
    answer = incoming[:, half:].reshape(nslot, levels, PATCH, cols)
    for_other = spread(recv_sel, KAPPA * arrived)
    for_mine = spread(send_sel, answer * jnp.tanh(sent))
    updated = mine + swap_sec(for_other) + for_mine
    return updated.reshape(levels, rows, cols)


def body(adjoint_state, forcing, viscosity, reaction, source_patch, owner, cavity_map):
    w = SWEEPS // 2
    levels, rows, cols = adjoint_state.shape[1:]
    invd = 1.0 / (4.0 * viscosity + reaction)
    stacked = jnp.concatenate([adjoint_state[0], forcing[0], viscosity, invd], axis=0)
    ext = halo(stacked, w)
    field = ext[:levels]
    force = ext[levels:2 * levels]
    visc = ext[2 * levels:2 * levels + 1]
    inv_wide = ext[2 * levels + 1:]
    sel = selectors(source_patch, owner, cavity_map, rows // PATCH)
    x1 = sweeps(field, visc, inv_wide, force, w, rows, cols)
    x2 = couple(x1, sel)
    out = sweeps(halo(x2, w), visc, inv_wide, force, SWEEPS - w, rows, cols)
    return out[None]


def solution(mesh):
    return jax.shard_map(
        body,
        mesh=mesh,
        in_specs=(
            P("sec", None, "gx", "gy"),
            P("sec", None, "gx", "gy"),
            P("sec", "gx", "gy"),
            P("sec", "gx", "gy"),
            P("sec", ("gx", "gy")),
            P("sec", ("gx", "gy"), None),
            P("sec", ("gx", "gy"), None, None),
        ),
        out_specs=P("sec", None, "gx", "gy"),
        check_vma=False,
    )
```

```python
import jax
import jax.numpy as jnp
from jax import lax
from jax.sharding import PartitionSpec as P
from jax.experimental import pallas as pl
from jax.experimental.pallas import tpu as pltpu

PATCH = 2
PW = 128
SWEEPS = 8


OMEGA = 0.8
KAPPA = 0.5
HIGHEST = lax.Precision.HIGHEST


def shifted(block, dx, dy):
    nx = lax.axis_size("gx")
    ny = lax.axis_size("gy")
    pairs = []
    for a in range(nx):
        for b in range(ny):
            sa, sb = a + dx, b + dy
            if 0 <= sa < nx and 0 <= sb < ny:
                pairs.append((sa * ny + sb, a * ny + b))
    return lax.ppermute(block, ("gx", "gy"), pairs)


def halo(cells, w):
    chans, rows, cols = cells.shape
    west = shifted(cells[:, :, -w:], 0, -1)
    east = shifted(cells[:, :, :w], 0, 1)
    gap = jnp.zeros((chans, rows, cols - 2 * w), cells.dtype)
    wide = jnp.concatenate([cells, east, gap, west], axis=2)
    north = shifted(wide[:, -w:], -1, 0)
    south = shifted(wide[:, :w], 1, 0)
    return jnp.concatenate([wide, south, north], axis=1)


def sweeps(ext, force, count, rows, cols):
    levels = ext.shape[0] if force is not None else (ext.shape[0] - 2) // 2
    height, lanes = ext.shape[1:]
    vmem = pl.BlockSpec(memory_space=pltpu.VMEM)

    def kernel(x_ref, f_ref, o_ref):
        if force is None:
            f_ref = x_ref
        nf = f_ref.shape[0]
        scale = OMEGA * f_ref[nf - 1]
        visc = f_ref[nf - 2]
        base = nf - 2 - levels

        def level(l, carry):
            x = x_ref[l]
            f = f_ref[base + l]
            for _ in range(count):
                beside = pltpu.roll(x, 1, 0) + pltpu.roll(x, height - 1, 0)
                beside = beside + pltpu.roll(x, 1, 1) + pltpu.roll(x, lanes - 1, 1)
                x = (1.0 - OMEGA) * x + scale * (f + visc * beside)
            o_ref[l] = x[:rows, :cols]
            return carry

        lax.fori_loop(0, levels, level, 0)

    side = ext if force is None else force
    return pl.pallas_call(
        kernel,
        out_shape=jax.ShapeDtypeStruct((levels, rows, cols), jnp.float32),
        in_specs=[vmem, vmem],
        out_specs=vmem,
    )(ext, side)


def swap_sec(x):
    return lax.ppermute(x, "sec", [(0, 1), (1, 0)])


def onehot(index, size):
    return (index[:, None] == jnp.arange(size, dtype=jnp.int32)[None, :]).astype(jnp.float32)


def pick(sel, patches):
    return jnp.einsum("jk,lkrc->jlrc", sel, patches, precision=HIGHEST)


def spread(sel, values):
    return jnp.einsum("jk,jlrc->lkrc", sel, values, precision=HIGHEST)


def selectors(source_patch, owner, cavity_map, npatch):
    groups, slots_per = cavity_map.shape[2], cavity_map.shape[3]
    nslot = groups * slots_per
    sources = source_patch[0]
    dest = owner[0, :, 0]
    count = dest.shape[0]
    earlier = jnp.arange(count)[None, :] < jnp.arange(count)[:, None]
    rank = jnp.sum((dest[:, None] == dest[None, :]) & earlier, axis=1).astype(jnp.int32)
    slot = dest * slots_per + rank
    send_sel = jnp.dot(onehot(slot, nslot).T, onehot(sources, npatch), precision=HIGHEST)
    cav_other = swap_sec(cavity_map[0, 0].reshape(-1))
    recv_sel = onehot(cav_other, npatch)
    return send_sel, recv_sel, groups, slots_per


def couple(x1, sel):
    send_sel, recv_sel, groups, slots_per = sel
    levels, rows, cols = x1.shape
    npatch = rows // PATCH
    nslot = groups * slots_per
    mine = x1.reshape(levels, npatch, PATCH, cols)
    other = swap_sec(mine)
    sent = pick(send_sel, mine)
    local = pick(recv_sel, other)
    half = slots_per * levels * PATCH
    chunk = (groups, half, cols)
    outgoing = jnp.concatenate([sent.reshape(chunk), local.reshape(chunk)], axis=1)
    incoming = lax.all_to_all(outgoing, ("gx", "gy"), 0, 0, tiled=True)
    arrived = incoming[:, :half].reshape(nslot, levels, PATCH, cols)
    answer = incoming[:, half:].reshape(nslot, levels, PATCH, cols)
    for_other = spread(recv_sel, KAPPA * arrived)
    for_mine = spread(send_sel, answer * jnp.tanh(sent))
    updated = mine + swap_sec(for_other) + for_mine
    return updated.reshape(levels, rows, cols)


def body(adjoint_state, forcing, viscosity, reaction, source_patch, owner, cavity_map):
    w = SWEEPS // 2
    levels, rows, cols = adjoint_state.shape[1:]
    invd = 1.0 / (4.0 * viscosity + reaction)
    stacked = jnp.concatenate([adjoint_state[0], forcing[0], viscosity, invd], axis=0)
    ext = halo(stacked, w)
    sel = selectors(source_patch, owner, cavity_map, rows // PATCH)
    x1 = sweeps(ext, None, w, rows, cols)
    x2 = couple(x1, sel)
    out = sweeps(halo(x2, w), ext, SWEEPS - w, rows, cols)
    return out[None]


def solution(mesh):
    return jax.shard_map(
        body,
        mesh=mesh,
        in_specs=(
            P("sec", None, "gx", "gy"),
            P("sec", None, "gx", "gy"),
            P("sec", "gx", "gy"),
            P("sec", "gx", "gy"),
            P("sec", ("gx", "gy")),
            P("sec", ("gx", "gy"), None),
            P("sec", ("gx", "gy"), None, None),
        ),
        out_specs=P("sec", None, "gx", "gy"),
        check_vma=False,
    )
```

```python
import jax
import jax.numpy as jnp
from jax import lax
from jax.sharding import PartitionSpec as P
from jax.experimental import pallas as pl
from jax.experimental.pallas import tpu as pltpu

PATCH = 2
PW = 128
SWEEPS = 8


OMEGA = 0.8
KAPPA = 0.5
HIGHEST = lax.Precision.HIGHEST


def shifted(block, dx, dy):
    nx = lax.axis_size("gx")
    ny = lax.axis_size("gy")
    pairs = []
    for a in range(nx):
        for b in range(ny):
            sa, sb = a + dx, b + dy
            if 0 <= sa < nx and 0 <= sb < ny:
                pairs.append((sa * ny + sb, a * ny + b))
    return lax.ppermute(block, ("gx", "gy"), pairs)


def halo(cells, w):
    chans, rows, cols = cells.shape
    west = shifted(cells[:, :, -w:], 0, -1)
    east = shifted(cells[:, :, :w], 0, 1)
    gap = jnp.zeros((chans, rows, cols - 2 * w), cells.dtype)
    wide = jnp.concatenate([cells, east, gap, west], axis=2)
    north = shifted(wide[:, -w:], -1, 0)
    south = shifted(wide[:, :w], 1, 0)
    return jnp.concatenate([north, wide, south], axis=1)


def sweeps(ext, force, count, rows, cols):
    levels = ext.shape[0] if force is not None else (ext.shape[0] - 2) // 2
    height, lanes = ext.shape[1:]
    w = (height - rows) // 2
    pad = 8
    vmem = pl.BlockSpec(memory_space=pltpu.VMEM)

    def kernel(x_ref, f_ref, o_ref, s_ref):
        if force is None:
            f_ref = x_ref
        nf = f_ref.shape[0]
        scale = OMEGA * f_ref[nf - 1]
        visc = f_ref[nf - 2]
        base = nf - 2 - levels
        s_ref[0:pad] = jnp.zeros((pad, lanes), jnp.float32)
        s_ref[pad + height:] = jnp.zeros((pad, lanes), jnp.float32)

        def level(l, carry):
            x = x_ref[l]
            f = f_ref[base + l]
            for _ in range(count):
                s_ref[pad:pad + height] = x
                beside = s_ref[pad + 1:pad + 1 + height] + s_ref[pad - 1:pad - 1 + height]
                beside = beside + pltpu.roll(x, lanes - 1, 1) + pltpu.roll(x, 1, 1)
                x = (1.0 - OMEGA) * x + scale * (f + visc * beside)
            s_ref[pad:pad + height] = x
            o_ref[l] = s_ref[pad + w:pad + w + rows, 0:cols]
            return carry

        lax.fori_loop(0, levels, level, 0)

    side = ext if force is None else force
    return pl.pallas_call(
        kernel,
        out_shape=jax.ShapeDtypeStruct((levels, rows, cols), jnp.float32),
        in_specs=[vmem, vmem],
        out_specs=vmem,
        scratch_shapes=[pltpu.VMEM((height + 2 * pad, lanes), jnp.float32)],
    )(ext, side)


def swap_sec(x):
    return lax.ppermute(x, "sec", [(0, 1), (1, 0)])


def onehot(index, size):
    return (index[:, None] == jnp.arange(size, dtype=jnp.int32)[None, :]).astype(jnp.float32)


def pick(sel, patches):
    return jnp.einsum("jk,lkrc->jlrc", sel, patches, precision=HIGHEST)


def spread(sel, values):
    return jnp.einsum("jk,jlrc->lkrc", sel, values, precision=HIGHEST)


def selectors(source_patch, owner, cavity_map, npatch):
    groups, slots_per = cavity_map.shape[2], cavity_map.shape[3]
    nslot = groups * slots_per
    sources = source_patch[0]
    dest = owner[0, :, 0]
    count = dest.shape[0]
    earlier = jnp.arange(count)[None, :] < jnp.arange(count)[:, None]
    rank = jnp.sum((dest[:, None] == dest[None, :]) & earlier, axis=1).astype(jnp.int32)
    slot = dest * slots_per + rank
    send_sel = jnp.dot(onehot(slot, nslot).T, onehot(sources, npatch), precision=HIGHEST)
    cav_other = swap_sec(cavity_map[0, 0].reshape(-1))
    recv_sel = onehot(cav_other, npatch)
    return send_sel, recv_sel, groups, slots_per


def couple(x1, sel):
    send_sel, recv_sel, groups, slots_per = sel
    levels, rows, cols = x1.shape
    npatch = rows // PATCH
    nslot = groups * slots_per
    mine = x1.reshape(levels, npatch, PATCH, cols)
    other = swap_sec(mine)
    sent = pick(send_sel, mine)
    local = pick(recv_sel, other)
    half = slots_per * levels * PATCH
    chunk = (groups, half, cols)
    outgoing = jnp.concatenate([sent.reshape(chunk), local.reshape(chunk)], axis=1)
    incoming = lax.all_to_all(outgoing, ("gx", "gy"), 0, 0, tiled=True)
    arrived = incoming[:, :half].reshape(nslot, levels, PATCH, cols)
    answer = incoming[:, half:].reshape(nslot, levels, PATCH, cols)
    for_other = spread(recv_sel, KAPPA * arrived)
    for_mine = spread(send_sel, answer * jnp.tanh(sent))
    updated = mine + swap_sec(for_other) + for_mine
    return updated.reshape(levels, rows, cols)


def body(adjoint_state, forcing, viscosity, reaction, source_patch, owner, cavity_map):
    w = SWEEPS // 2
    levels, rows, cols = adjoint_state.shape[1:]
    invd = 1.0 / (4.0 * viscosity + reaction)
    stacked = jnp.concatenate([adjoint_state[0], forcing[0], viscosity, invd], axis=0)
    ext = halo(stacked, w)
    sel = selectors(source_patch, owner, cavity_map, rows // PATCH)
    x1 = sweeps(ext, None, w, rows, cols)
    x2 = couple(x1, sel)
    out = sweeps(halo(x2, w), ext, SWEEPS - w, rows, cols)
    return out[None]


def solution(mesh):
    return jax.shard_map(
        body,
        mesh=mesh,
        in_specs=(
            P("sec", None, "gx", "gy"),
            P("sec", None, "gx", "gy"),
            P("sec", "gx", "gy"),
            P("sec", "gx", "gy"),
            P("sec", ("gx", "gy")),
            P("sec", ("gx", "gy"), None),
            P("sec", ("gx", "gy"), None, None),
        ),
        out_specs=P("sec", None, "gx", "gy"),
        check_vma=False,
    )
```

```python
import jax
import jax.numpy as jnp
from jax import lax
from jax.sharding import PartitionSpec as P

PATCH = 2
PW = 128
SWEEPS = 8


OMEGA = 0.8
KAPPA = 0.5
HIGHEST = lax.Precision.HIGHEST


def shifted(block, dx, dy):
    nx = lax.axis_size("gx")
    ny = lax.axis_size("gy")
    pairs = []
    for a in range(nx):
        for b in range(ny):
            sa, sb = a + dx, b + dy
            if 0 <= sa < nx and 0 <= sb < ny:
                pairs.append((sa * ny + sb, a * ny + b))
    return lax.ppermute(block, ("gx", "gy"), pairs)


def halo(cells, w):
    west = shifted(cells[:, :, -w:], 0, -1)
    east = shifted(cells[:, :, :w], 0, 1)
    wide = jnp.concatenate([west, cells, east], axis=2)
    north = shifted(wide[:, -w:], -1, 0)
    south = shifted(wide[:, :w], 1, 0)
    return jnp.concatenate([north, wide, south], axis=1)


def relax(field, visc, invd, force):
    padded = jnp.pad(field, ((0, 0), (1, 1), (1, 1)))
    beside = padded[:, 2:, 1:-1] + padded[:, :-2, 1:-1]
    beside = beside + padded[:, 1:-1, 2:] + padded[:, 1:-1, :-2]
    return (1.0 - OMEGA) * field + OMEGA * invd * (force + visc * beside)


def sweeps(ext, visc, invd, force, count, w):
    for _ in range(count):
        ext = relax(ext, visc, invd, force)
    return ext[:, w:-w, w:-w]


def swap_sec(x):
    return lax.ppermute(x, "sec", [(0, 1), (1, 0)])


def onehot(index, size):
    return (index[:, None] == jnp.arange(size, dtype=jnp.int32)[None, :]).astype(jnp.float32)


def pick(sel, patches):
    return jnp.einsum("jk,lrkc->jlrc", sel, patches, precision=HIGHEST)


def spread(sel, values):
    return jnp.einsum("jk,jlrc->lrkc", sel, values, precision=HIGHEST)


def selectors(source_patch, owner, cavity_map, npatch):
    groups, slots_per = cavity_map.shape[2], cavity_map.shape[3]
    nslot = groups * slots_per
    sources = source_patch[0]
    dest = owner[0, :, 0]
    count = dest.shape[0]
    earlier = jnp.arange(count)[None, :] < jnp.arange(count)[:, None]
    rank = jnp.sum((dest[:, None] == dest[None, :]) & earlier, axis=1).astype(jnp.int32)
    slot = dest * slots_per + rank
    send_sel = jnp.dot(onehot(slot, nslot).T, onehot(sources, npatch), precision=HIGHEST)
    cav_other = swap_sec(cavity_map[0, 0].reshape(-1))
    recv_sel = onehot(cav_other, npatch)
    return send_sel, recv_sel, groups, slots_per


def couple(x1, sel):
    send_sel, recv_sel, groups, slots_per = sel
    levels, rows, cols = x1.shape
    npatch = rows // PATCH
    nslot = groups * slots_per
    mine = x1.reshape(levels, npatch, PATCH, cols).transpose(0, 2, 1, 3)
    other = swap_sec(mine)
    sent = pick(send_sel, mine)
    local = pick(recv_sel, other)
    half = slots_per * levels * PATCH
    chunk = (groups, half, cols)
    outgoing = jnp.concatenate([sent.reshape(chunk), local.reshape(chunk)], axis=1)
    incoming = lax.all_to_all(outgoing, ("gx", "gy"), 0, 0, tiled=True)
    arrived = incoming[:, :half].reshape(nslot, levels, PATCH, cols)
    answer = incoming[:, half:].reshape(nslot, levels, PATCH, cols)
    for_other = spread(recv_sel, KAPPA * arrived)
    for_mine = spread(send_sel, answer * jnp.tanh(sent))
    updated = mine + swap_sec(for_other) + for_mine
    return updated.transpose(0, 2, 1, 3).reshape(levels, rows, cols)


def body(adjoint_state, forcing, viscosity, reaction, source_patch, owner, cavity_map):
    w = SWEEPS // 2
    levels, rows, cols = adjoint_state.shape[1:]
    invd = 1.0 / (4.0 * viscosity + reaction)
    stacked = jnp.concatenate([adjoint_state[0], forcing[0], viscosity, invd], axis=0)
    ext = halo(stacked, w)
    field = ext[:levels]
    force = ext[levels:2 * levels]
    visc = ext[2 * levels:2 * levels + 1]
    inv_wide = ext[2 * levels + 1:]
    sel = selectors(source_patch, owner, cavity_map, rows // PATCH)
    x1 = sweeps(field, visc, inv_wide, force, w, w)
    x2 = couple(x1, sel)
    out = sweeps(halo(x2, w), visc, inv_wide, force, SWEEPS - w, w)
    return out[None]


def solution(mesh):
    return jax.shard_map(
        body,
        mesh=mesh,
        in_specs=(
            P("sec", None, "gx", "gy"),
            P("sec", None, "gx", "gy"),
            P("sec", "gx", "gy"),
            P("sec", "gx", "gy"),
            P("sec", ("gx", "gy")),
            P("sec", ("gx", "gy"), None),
            P("sec", ("gx", "gy"), None, None),
        ),
        out_specs=P("sec", None, "gx", "gy"),
        check_vma=False,
    )
```

```python
import jax
import jax.numpy as jnp
from jax import lax
from jax.sharding import PartitionSpec as P

PATCH = 2
PW = 128
SWEEPS = 8


OMEGA = 0.8
KAPPA = 0.5
HIGHEST = lax.Precision.HIGHEST


def shifted(block, dx, dy):
    nx = lax.axis_size("gx")
    ny = lax.axis_size("gy")
    pairs = []
    for a in range(nx):
        for b in range(ny):
            sa, sb = a + dx, b + dy
            if 0 <= sa < nx and 0 <= sb < ny:
                pairs.append((sa * ny + sb, a * ny + b))
    return lax.ppermute(block, ("gx", "gy"), pairs)


def halo(cells, w):
    west = shifted(cells[:, :, -w:], 0, -1)
    east = shifted(cells[:, :, :w], 0, 1)
    wide = jnp.concatenate([west, cells, east], axis=2)
    north = shifted(wide[:, -w:], -1, 0)
    south = shifted(wide[:, :w], 1, 0)
    return jnp.concatenate([north, wide, south], axis=1)


def relax(field, visc, invd, force):
    padded = jnp.pad(field, ((0, 0), (1, 1), (1, 1)))
    beside = padded[:, 2:, 1:-1] + padded[:, :-2, 1:-1]
    beside = beside + padded[:, 1:-1, 2:] + padded[:, 1:-1, :-2]
    return (1.0 - OMEGA) * field + OMEGA * invd * (force + visc * beside)


def sweeps(ext, visc, invd, force, count, w):
    for _ in range(count - 1):
        ext = relax(ext, visc, invd, force)
    inner = (slice(None), slice(w, -w), slice(w, -w))
    beside = ext[:, w + 1:-w + 1, w:-w] + ext[:, w - 1:-w - 1, w:-w]
    beside = beside + ext[:, w:-w, w + 1:-w + 1] + ext[:, w:-w, w - 1:-w - 1]
    return (1.0 - OMEGA) * ext[inner] + OMEGA * invd[inner] * (force[inner] + visc[inner] * beside)


def swap_sec(x):
    return lax.ppermute(x, "sec", [(0, 1), (1, 0)])


def onehot(index, size):
    return (index[:, None] == jnp.arange(size, dtype=jnp.int32)[None, :]).astype(jnp.float32)


def pick(sel, patches):
    return jnp.einsum("jk,lkrc->jlrc", sel, patches, precision=HIGHEST)


def spread(sel, values):
    return jnp.einsum("jk,jlrc->lkrc", sel, values, precision=HIGHEST)


def selectors(source_patch, owner, cavity_map, npatch):
    groups, slots_per = cavity_map.shape[2], cavity_map.shape[3]
    nslot = groups * slots_per
    sources = source_patch[0]
    dest = owner[0, :, 0]
    count = dest.shape[0]
    earlier = jnp.arange(count)[None, :] < jnp.arange(count)[:, None]
    rank = jnp.sum((dest[:, None] == dest[None, :]) & earlier, axis=1).astype(jnp.int32)
    slot = dest * slots_per + rank
    send_sel = jnp.dot(onehot(slot, nslot).T, onehot(sources, npatch), precision=HIGHEST)
    cav_other = swap_sec(cavity_map[0, 0].reshape(-1))
    recv_sel = onehot(cav_other, npatch)
    return send_sel, recv_sel, groups, slots_per


def couple(x1, sel):
    send_sel, recv_sel, groups, slots_per = sel
    levels, rows, cols = x1.shape
    npatch = rows // PATCH
    nslot = groups * slots_per
    mine = x1.reshape(levels, npatch, PATCH, cols)
    other = swap_sec(mine)
    sent = pick(send_sel, mine)
    local = pick(recv_sel, other)
    half = slots_per * levels * PATCH
    chunk = (groups, half, cols)
    outgoing = jnp.concatenate([sent.reshape(chunk), local.reshape(chunk)], axis=1)
    incoming = lax.all_to_all(outgoing, ("gx", "gy"), 0, 0, tiled=True)
    arrived = incoming[:, :half].reshape(nslot, levels, PATCH, cols)
    answer = incoming[:, half:].reshape(nslot, levels, PATCH, cols)
    for_other = spread(recv_sel, KAPPA * arrived)
    for_mine = spread(send_sel, answer * jnp.tanh(sent))
    updated = mine + swap_sec(for_other) + for_mine
    return updated.reshape(levels, rows, cols)


def body(adjoint_state, forcing, viscosity, reaction, source_patch, owner, cavity_map):
    w = SWEEPS // 2
    levels, rows, cols = adjoint_state.shape[1:]
    invd = 1.0 / (4.0 * viscosity + reaction)
    stacked = jnp.concatenate([adjoint_state[0], forcing[0], viscosity, invd], axis=0)
    ext = halo(stacked, w)
    field = ext[:levels]
    force = ext[levels:2 * levels]
    visc = ext[2 * levels:2 * levels + 1]
    inv_wide = ext[2 * levels + 1:]
    sel = selectors(source_patch, owner, cavity_map, rows // PATCH)
    x1 = sweeps(field, visc, inv_wide, force, w, w)
    x2 = couple(x1, sel)
    out = sweeps(halo(x2, w), visc, inv_wide, force, SWEEPS - w, w)
    return out[None]


def solution(mesh):
    return jax.shard_map(
        body,
        mesh=mesh,
        in_specs=(
            P("sec", None, "gx", "gy"),
            P("sec", None, "gx", "gy"),
            P("sec", "gx", "gy"),
            P("sec", "gx", "gy"),
            P("sec", ("gx", "gy")),
            P("sec", ("gx", "gy"), None),
            P("sec", ("gx", "gy"), None, None),
        ),
        out_specs=P("sec", None, "gx", "gy"),
        check_vma=False,
    )
```

```python
import jax
import jax.numpy as jnp
from jax import lax
from jax.sharding import PartitionSpec as P

PATCH = 2
PW = 128
SWEEPS = 8


OMEGA = 0.8
KAPPA = 0.5
HIGHEST = lax.Precision.HIGHEST


def shifted(block, dx, dy):
    nx = lax.axis_size("gx")
    ny = lax.axis_size("gy")
    pairs = []
    for a in range(nx):
        for b in range(ny):
            sa, sb = a + dx, b + dy
            if 0 <= sa < nx and 0 <= sb < ny:
                pairs.append((sa * ny + sb, a * ny + b))
    return lax.ppermute(block, ("gx", "gy"), pairs)


def halo(cells, w):
    west = shifted(cells[:, :, -w:], 0, -1)
    east = shifted(cells[:, :, :w], 0, 1)
    wide = jnp.concatenate([west, cells, east], axis=2)
    north = shifted(wide[:, -w:], -1, 0)
    south = shifted(wide[:, :w], 1, 0)
    return jnp.concatenate([north, wide, south], axis=1)


def relax(field, visc, invd, force):
    padded = jnp.pad(field, ((0, 0), (1, 1), (1, 1)))
    beside = padded[:, 2:, 1:-1] + padded[:, :-2, 1:-1]
    beside = beside + padded[:, 1:-1, 2:] + padded[:, 1:-1, :-2]
    return (1.0 - OMEGA) * field + OMEGA * invd * (force + visc * beside)


def sweeps(ext, visc, invd, force, count, w):
    height, width = ext.shape[1:]
    for k in range(1, count + 1):
        rows, cols = slice(k, height - k), slice(k, width - k)
        beside = ext[:, 2:, 1:-1] + ext[:, :-2, 1:-1]
        beside = beside + ext[:, 1:-1, 2:] + ext[:, 1:-1, :-2]
        center = ext[:, 1:-1, 1:-1]
        ext = (1.0 - OMEGA) * center + OMEGA * invd[:, rows, cols] * (force[:, rows, cols] + visc[:, rows, cols] * beside)
    return ext


def swap_sec(x):
    return lax.ppermute(x, "sec", [(0, 1), (1, 0)])


def onehot(index, size):
    return (index[:, None] == jnp.arange(size, dtype=jnp.int32)[None, :]).astype(jnp.float32)


def pick(sel, patches):
    return jnp.einsum("jk,lkrc->jlrc", sel, patches, precision=HIGHEST)


def spread(sel, values):
    return jnp.einsum("jk,jlrc->lkrc", sel, values, precision=HIGHEST)


def selectors(source_patch, owner, cavity_map, npatch):
    groups, slots_per = cavity_map.shape[2], cavity_map.shape[3]
    nslot = groups * slots_per
    sources = source_patch[0]
    dest = owner[0, :, 0]
    count = dest.shape[0]
    earlier = jnp.arange(count)[None, :] < jnp.arange(count)[:, None]
    rank = jnp.sum((dest[:, None] == dest[None, :]) & earlier, axis=1).astype(jnp.int32)
    slot = dest * slots_per + rank
    send_sel = jnp.dot(onehot(slot, nslot).T, onehot(sources, npatch), precision=HIGHEST)
    cav_other = swap_sec(cavity_map[0, 0].reshape(-1))
    recv_sel = onehot(cav_other, npatch)
    return send_sel, recv_sel, groups, slots_per


def couple(x1, sel):
    send_sel, recv_sel, groups, slots_per = sel
    levels, rows, cols = x1.shape
    npatch = rows // PATCH
    nslot = groups * slots_per
    mine = x1.reshape(levels, npatch, PATCH, cols)
    other = swap_sec(mine)
    sent = pick(send_sel, mine)
    local = pick(recv_sel, other)
    half = slots_per * levels * PATCH
    chunk = (groups, half, cols)
    outgoing = jnp.concatenate([sent.reshape(chunk), local.reshape(chunk)], axis=1)
    incoming = lax.all_to_all(outgoing, ("gx", "gy"), 0, 0, tiled=True)
    arrived = incoming[:, :half].reshape(nslot, levels, PATCH, cols)
    answer = incoming[:, half:].reshape(nslot, levels, PATCH, cols)
    for_other = spread(recv_sel, KAPPA * arrived)
    for_mine = spread(send_sel, answer * jnp.tanh(sent))
    updated = mine + swap_sec(for_other) + for_mine
    return updated.reshape(levels, rows, cols)


def body(adjoint_state, forcing, viscosity, reaction, source_patch, owner, cavity_map):
    w = SWEEPS // 2
    levels, rows, cols = adjoint_state.shape[1:]
    invd = 1.0 / (4.0 * viscosity + reaction)
    stacked = jnp.concatenate([adjoint_state[0], forcing[0], viscosity, invd], axis=0)
    ext = halo(stacked, w)
    field = ext[:levels]
    force = ext[levels:2 * levels]
    visc = ext[2 * levels:2 * levels + 1]
    inv_wide = ext[2 * levels + 1:]
    sel = selectors(source_patch, owner, cavity_map, rows // PATCH)
    x1 = sweeps(field, visc, inv_wide, force, w, w)
    x2 = couple(x1, sel)
    out = sweeps(halo(x2, w), visc, inv_wide, force, SWEEPS - w, w)
    return out[None]


def solution(mesh):
    return jax.shard_map(
        body,
        mesh=mesh,
        in_specs=(
            P("sec", None, "gx", "gy"),
            P("sec", None, "gx", "gy"),
            P("sec", "gx", "gy"),
            P("sec", "gx", "gy"),
            P("sec", ("gx", "gy")),
            P("sec", ("gx", "gy"), None),
            P("sec", ("gx", "gy"), None, None),
        ),
        out_specs=P("sec", None, "gx", "gy"),
        check_vma=False,
    )
```

```python
import jax
import jax.numpy as jnp
from jax import lax
from jax.sharding import PartitionSpec as P

PATCH = 2
PW = 128
SWEEPS = 8


OMEGA = 0.8
KAPPA = 0.5
HIGHEST = lax.Precision.HIGHEST


def shifted(block, dx, dy):
    nx = lax.axis_size("gx")
    ny = lax.axis_size("gy")
    pairs = []
    for a in range(nx):
        for b in range(ny):
            sa, sb = a + dx, b + dy
            if 0 <= sa < nx and 0 <= sb < ny:
                pairs.append((sa * ny + sb, a * ny + b))
    return lax.ppermute(block, ("gx", "gy"), pairs)


def columns(cells, start, w):
    sel = onehot(start + jnp.arange(w, dtype=jnp.int32), cells.shape[2])
    return jnp.einsum("jc,lrc->ljr", sel, cells, precision=HIGHEST)


def uncolumns(strips):
    return jnp.einsum("ljr,jm->lrm", strips, jnp.eye(strips.shape[1], dtype=strips.dtype), precision=HIGHEST)


def halo(cells, w):
    cols = cells.shape[2]
    west = uncolumns(shifted(columns(cells, cols - w, w), 0, -1))
    east = uncolumns(shifted(columns(cells, 0, w), 0, 1))
    wide = jnp.concatenate([west, cells, east], axis=2)
    north = shifted(wide[:, -w:], -1, 0)
    south = shifted(wide[:, :w], 1, 0)
    return jnp.concatenate([north, wide, south], axis=1)


def relax(field, visc, invd, force):
    padded = jnp.pad(field, ((0, 0), (1, 1), (1, 1)))
    beside = padded[:, 2:, 1:-1] + padded[:, :-2, 1:-1]
    beside = beside + padded[:, 1:-1, 2:] + padded[:, 1:-1, :-2]
    return (1.0 - OMEGA) * field + OMEGA * invd * (force + visc * beside)


def sweeps(ext, visc, invd, force, count, w):
    for _ in range(count - 1):
        ext = relax(ext, visc, invd, force)
    inner = (slice(None), slice(w, -w), slice(w, -w))
    beside = ext[:, w + 1:-w + 1, w:-w] + ext[:, w - 1:-w - 1, w:-w]
    beside = beside + ext[:, w:-w, w + 1:-w + 1] + ext[:, w:-w, w - 1:-w - 1]
    return (1.0 - OMEGA) * ext[inner] + OMEGA * invd[inner] * (force[inner] + visc[inner] * beside)


def swap_sec(x):
    return lax.ppermute(x, "sec", [(0, 1), (1, 0)])


def onehot(index, size):
    return (index[:, None] == jnp.arange(size, dtype=jnp.int32)[None, :]).astype(jnp.float32)


def pick(sel, patches):
    return jnp.einsum("jk,lkrc->jlrc", sel, patches, precision=HIGHEST)


def spread(sel, values):
    return jnp.einsum("jk,jlrc->lkrc", sel, values, precision=HIGHEST)


def selectors(source_patch, owner, cavity_map, npatch):
    groups, slots_per = cavity_map.shape[2], cavity_map.shape[3]
    nslot = groups * slots_per
    sources = source_patch[0]
    dest = owner[0, :, 0]
    count = dest.shape[0]
    earlier = jnp.arange(count)[None, :] < jnp.arange(count)[:, None]
    rank = jnp.sum((dest[:, None] == dest[None, :]) & earlier, axis=1).astype(jnp.int32)
    slot = dest * slots_per + rank
    send_sel = jnp.dot(onehot(slot, nslot).T, onehot(sources, npatch), precision=HIGHEST)
    cav_other = swap_sec(cavity_map[0, 0].reshape(-1))
    recv_sel = onehot(cav_other, npatch)
    return send_sel, recv_sel, groups, slots_per


def couple(x1, sel):
    send_sel, recv_sel, groups, slots_per = sel
    levels, rows, cols = x1.shape
    npatch = rows // PATCH
    nslot = groups * slots_per
    mine = x1.reshape(levels, npatch, PATCH, cols)
    other = swap_sec(mine)
    sent = pick(send_sel, mine)
    local = pick(recv_sel, other)
    half = slots_per * levels * PATCH
    chunk = (groups, half, cols)
    outgoing = jnp.concatenate([sent.reshape(chunk), local.reshape(chunk)], axis=1)
    incoming = lax.all_to_all(outgoing, ("gx", "gy"), 0, 0, tiled=True)
    arrived = incoming[:, :half].reshape(nslot, levels, PATCH, cols)
    answer = incoming[:, half:].reshape(nslot, levels, PATCH, cols)
    for_other = spread(recv_sel, KAPPA * arrived)
    for_mine = spread(send_sel, answer * jnp.tanh(sent))
    updated = mine + swap_sec(for_other) + for_mine
    return updated.reshape(levels, rows, cols)


def body(adjoint_state, forcing, viscosity, reaction, source_patch, owner, cavity_map):
    w = SWEEPS // 2
    levels, rows, cols = adjoint_state.shape[1:]
    invd = 1.0 / (4.0 * viscosity + reaction)
    stacked = jnp.concatenate([adjoint_state[0], forcing[0], viscosity, invd], axis=0)
    ext = halo(stacked, w)
    field = ext[:levels]
    force = ext[levels:2 * levels]
    visc = ext[2 * levels:2 * levels + 1]
    inv_wide = ext[2 * levels + 1:]
    sel = selectors(source_patch, owner, cavity_map, rows // PATCH)
    x1 = sweeps(field, visc, inv_wide, force, w, w)
    x2 = couple(x1, sel)
    out = sweeps(halo(x2, w), visc, inv_wide, force, SWEEPS - w, w)
    return out[None]


def solution(mesh):
    return jax.shard_map(
        body,
        mesh=mesh,
        in_specs=(
            P("sec", None, "gx", "gy"),
            P("sec", None, "gx", "gy"),
            P("sec", "gx", "gy"),
            P("sec", "gx", "gy"),
            P("sec", ("gx", "gy")),
            P("sec", ("gx", "gy"), None),
            P("sec", ("gx", "gy"), None, None),
        ),
        out_specs=P("sec", None, "gx", "gy"),
        check_vma=False,
    )
```

```python
import jax
import jax.numpy as jnp
from jax import lax
from jax.sharding import PartitionSpec as P

PATCH = 2
PW = 128
SWEEPS = 8


OMEGA = 0.8
KAPPA = 0.5
HIGHEST = lax.Precision.HIGHEST


def shifted(block, dx, dy):
    nx = lax.axis_size("gx")
    ny = lax.axis_size("gy")
    pairs = []
    for a in range(nx):
        for b in range(ny):
            sa, sb = a + dx, b + dy
            if 0 <= sa < nx and 0 <= sb < ny:
                pairs.append((sa * ny + sb, a * ny + b))
    return lax.ppermute(block, ("gx", "gy"), pairs)


def columns(cells, start, w):
    sel = onehot(start + jnp.arange(w, dtype=jnp.int32), cells.shape[2])
    return jnp.einsum("jc,lrc->ljr", sel, cells, precision=HIGHEST)


def uncolumns(strips):
    return jnp.einsum("ljr,jm->lrm", strips, jnp.eye(strips.shape[1], dtype=strips.dtype), precision=HIGHEST)


def halo(cells, w, right=None, left=None):
    cols = cells.shape[2]
    if right is None:
        right, left = columns(cells, cols - w, w), columns(cells, 0, w)
    west = uncolumns(shifted(right, 0, -1))
    east = uncolumns(shifted(left, 0, 1))
    wide = jnp.concatenate([west, cells, east], axis=2)
    north = shifted(wide[:, -w:], -1, 0)
    south = shifted(wide[:, :w], 1, 0)
    return jnp.concatenate([north, wide, south], axis=1)


def relax(field, visc, invd, force):
    padded = jnp.pad(field, ((0, 0), (1, 1), (1, 1)))
    beside = padded[:, 2:, 1:-1] + padded[:, :-2, 1:-1]
    beside = beside + padded[:, 1:-1, 2:] + padded[:, 1:-1, :-2]
    return (1.0 - OMEGA) * field + OMEGA * invd * (force + visc * beside)


def sweeps(ext, visc, invd, force, count, w):
    for _ in range(count - 1):
        ext = relax(ext, visc, invd, force)
    inner = (slice(None), slice(w, -w), slice(w, -w))
    beside = ext[:, w + 1:-w + 1, w:-w] + ext[:, w - 1:-w - 1, w:-w]
    beside = beside + ext[:, w:-w, w + 1:-w + 1] + ext[:, w:-w, w - 1:-w - 1]
    return (1.0 - OMEGA) * ext[inner] + OMEGA * invd[inner] * (force[inner] + visc[inner] * beside)


def swap_sec(x):
    return lax.ppermute(x, "sec", [(0, 1), (1, 0)])


def onehot(index, size):
    return (index[:, None] == jnp.arange(size, dtype=jnp.int32)[None, :]).astype(jnp.float32)


def pick(sel, patches):
    return jnp.einsum("jk,lkrc->jlrc", sel, patches, precision=HIGHEST)


def spread(sel, values):
    return jnp.einsum("jk,jlrc->lkrc", sel, values, precision=HIGHEST)


def selectors(source_patch, owner, cavity_map, npatch):
    groups, slots_per = cavity_map.shape[2], cavity_map.shape[3]
    nslot = groups * slots_per
    sources = source_patch[0]
    dest = owner[0, :, 0]
    count = dest.shape[0]
    earlier = jnp.arange(count)[None, :] < jnp.arange(count)[:, None]
    rank = jnp.sum((dest[:, None] == dest[None, :]) & earlier, axis=1).astype(jnp.int32)
    slot = dest * slots_per + rank
    send_sel = jnp.dot(onehot(slot, nslot).T, onehot(sources, npatch), precision=HIGHEST)
    cav_other = swap_sec(cavity_map[0, 0].reshape(-1))
    recv_sel = onehot(cav_other, npatch)
    return send_sel, recv_sel, groups, slots_per


def couple(x1, sel):
    send_sel, recv_sel, groups, slots_per = sel
    levels, rows, cols = x1.shape
    npatch = rows // PATCH
    nslot = groups * slots_per
    mine = x1.reshape(levels, npatch, PATCH, cols)
    other = swap_sec(mine)
    sent = pick(send_sel, mine)
    local = pick(recv_sel, other)
    half = slots_per * levels * PATCH
    chunk = (groups, half, cols)
    outgoing = jnp.concatenate([sent.reshape(chunk), local.reshape(chunk)], axis=1)
    incoming = lax.all_to_all(outgoing, ("gx", "gy"), 0, 0, tiled=True)
    arrived = incoming[:, :half].reshape(nslot, levels, PATCH, cols)
    answer = incoming[:, half:].reshape(nslot, levels, PATCH, cols)
    for_other = spread(recv_sel, KAPPA * arrived)
    for_mine = spread(send_sel, answer * jnp.tanh(sent))
    updated = mine + swap_sec(for_other) + for_mine
    return updated.reshape(levels, rows, cols)


def body(adjoint_state, forcing, viscosity, reaction, source_patch, owner, cavity_map):
    w = SWEEPS // 2
    levels, rows, cols = adjoint_state.shape[1:]
    invd = 1.0 / (4.0 * viscosity + reaction)
    stacked = jnp.concatenate([adjoint_state[0], forcing[0], viscosity, invd], axis=0)
    parts = [adjoint_state[0], forcing[0], viscosity, invd]
    right = jnp.concatenate([columns(p, cols - w, w) for p in parts], axis=0)
    left = jnp.concatenate([columns(p, 0, w) for p in parts], axis=0)
    ext = halo(stacked, w, right, left)
    field = ext[:levels]
    force = ext[levels:2 * levels]
    visc = ext[2 * levels:2 * levels + 1]
    inv_wide = ext[2 * levels + 1:]
    sel = selectors(source_patch, owner, cavity_map, rows // PATCH)
    x1 = sweeps(field, visc, inv_wide, force, w, w)
    x2 = couple(x1, sel)
    out = sweeps(halo(x2, w), visc, inv_wide, force, SWEEPS - w, w)
    return out[None]


def solution(mesh):
    return jax.shard_map(
        body,
        mesh=mesh,
        in_specs=(
            P("sec", None, "gx", "gy"),
            P("sec", None, "gx", "gy"),
            P("sec", "gx", "gy"),
            P("sec", "gx", "gy"),
            P("sec", ("gx", "gy")),
            P("sec", ("gx", "gy"), None),
            P("sec", ("gx", "gy"), None, None),
        ),
        out_specs=P("sec", None, "gx", "gy"),
        check_vma=False,
    )
```

```python
import jax
import jax.numpy as jnp
from jax import lax
from jax.sharding import PartitionSpec as P

PATCH = 2
PW = 128
SWEEPS = 8


OMEGA = 0.8
KAPPA = 0.5
HIGHEST = lax.Precision.HIGHEST


def shifted(block, dx, dy):
    nx = lax.axis_size("gx")
    ny = lax.axis_size("gy")
    pairs = []
    for a in range(nx):
        for b in range(ny):
            sa, sb = a + dx, b + dy
            if 0 <= sa < nx and 0 <= sb < ny:
                pairs.append((sa * ny + sb, a * ny + b))
    return lax.ppermute(block, ("gx", "gy"), pairs)


def columns(cells, start, w):
    sel = onehot(start + jnp.arange(w, dtype=jnp.int32), cells.shape[2])
    return jnp.einsum("jc,lrc->ljr", sel, cells, precision=HIGHEST)


def uncolumns(strips):
    return jnp.einsum("ljr,jm->lrm", strips, jnp.eye(strips.shape[1], dtype=strips.dtype), precision=HIGHEST)


def halo(cells, w):
    cols = cells.shape[2]
    index = jnp.concatenate([jnp.arange(cols - w, cols, dtype=jnp.int32), jnp.arange(w, dtype=jnp.int32)])
    both = jnp.einsum("jc,lrc->ljr", onehot(index, cols), cells, precision=HIGHEST)
    west = uncolumns(shifted(both[:, :w], 0, -1))
    east = uncolumns(shifted(both[:, w:], 0, 1))
    wide = jnp.concatenate([west, cells, east], axis=2)
    north = shifted(wide[:, -w:], -1, 0)
    south = shifted(wide[:, :w], 1, 0)
    return jnp.concatenate([north, wide, south], axis=1)


def relax(field, visc, invd, force):
    padded = jnp.pad(field, ((0, 0), (1, 1), (1, 1)))
    beside = padded[:, 2:, 1:-1] + padded[:, :-2, 1:-1]
    beside = beside + padded[:, 1:-1, 2:] + padded[:, 1:-1, :-2]
    return (1.0 - OMEGA) * field + OMEGA * invd * (force + visc * beside)


def sweeps(ext, visc, invd, force, count, w):
    for _ in range(count - 1):
        ext = relax(ext, visc, invd, force)
    inner = (slice(None), slice(w, -w), slice(w, -w))
    beside = ext[:, w + 1:-w + 1, w:-w] + ext[:, w - 1:-w - 1, w:-w]
    beside = beside + ext[:, w:-w, w + 1:-w + 1] + ext[:, w:-w, w - 1:-w - 1]
    return (1.0 - OMEGA) * ext[inner] + OMEGA * invd[inner] * (force[inner] + visc[inner] * beside)


def swap_sec(x):
    return lax.ppermute(x, "sec", [(0, 1), (1, 0)])


def onehot(index, size):
    return (index[:, None] == jnp.arange(size, dtype=jnp.int32)[None, :]).astype(jnp.float32)


def pick(sel, patches):
    return jnp.einsum("jk,lkrc->jlrc", sel, patches, precision=HIGHEST)


def spread(sel, values):
    return jnp.einsum("jk,jlrc->lkrc", sel, values, precision=HIGHEST)


def selectors(source_patch, owner, cavity_map, npatch):
    groups, slots_per = cavity_map.shape[2], cavity_map.shape[3]
    nslot = groups * slots_per
    sources = source_patch[0]
    dest = owner[0, :, 0]
    count = dest.shape[0]
    earlier = jnp.arange(count)[None, :] < jnp.arange(count)[:, None]
    rank = jnp.sum((dest[:, None] == dest[None, :]) & earlier, axis=1).astype(jnp.int32)
    slot = dest * slots_per + rank
    send_sel = jnp.dot(onehot(slot, nslot).T, onehot(sources, npatch), precision=HIGHEST)
    cav_other = swap_sec(cavity_map[0, 0].reshape(-1))
    recv_sel = onehot(cav_other, npatch)
    return send_sel, recv_sel, groups, slots_per


def couple(x1, sel):
    send_sel, recv_sel, groups, slots_per = sel
    levels, rows, cols = x1.shape
    npatch = rows // PATCH
    nslot = groups * slots_per
    mine = x1.reshape(levels, npatch, PATCH, cols)
    other = swap_sec(mine)
    sent = pick(send_sel, mine)
    local = pick(recv_sel, other)
    half = slots_per * levels * PATCH
    chunk = (groups, half, cols)
    outgoing = jnp.concatenate([sent.reshape(chunk), local.reshape(chunk)], axis=1)
    incoming = lax.all_to_all(outgoing, ("gx", "gy"), 0, 0, tiled=True)
    arrived = incoming[:, :half].reshape(nslot, levels, PATCH, cols)
    answer = incoming[:, half:].reshape(nslot, levels, PATCH, cols)
    for_other = spread(recv_sel, KAPPA * arrived)
    for_mine = spread(send_sel, answer * jnp.tanh(sent))
    updated = mine + swap_sec(for_other) + for_mine
    return updated.reshape(levels, rows, cols)


def body(adjoint_state, forcing, viscosity, reaction, source_patch, owner, cavity_map):
    w = SWEEPS // 2
    levels, rows, cols = adjoint_state.shape[1:]
    invd = 1.0 / (4.0 * viscosity + reaction)
    stacked = jnp.concatenate([adjoint_state[0], forcing[0], viscosity, invd], axis=0)
    ext = halo(stacked, w)
    field = ext[:levels]
    force = ext[levels:2 * levels]
    visc = ext[2 * levels:2 * levels + 1]
    inv_wide = ext[2 * levels + 1:]
    sel = selectors(source_patch, owner, cavity_map, rows // PATCH)
    x1 = sweeps(field, visc, inv_wide, force, w, w)
    x2 = couple(x1, sel)
    out = sweeps(halo(x2, w), visc, inv_wide, force, SWEEPS - w, w)
    return out[None]


def solution(mesh):
    return jax.shard_map(
        body,
        mesh=mesh,
        in_specs=(
            P("sec", None, "gx", "gy"),
            P("sec", None, "gx", "gy"),
            P("sec", "gx", "gy"),
            P("sec", "gx", "gy"),
            P("sec", ("gx", "gy")),
            P("sec", ("gx", "gy"), None),
            P("sec", ("gx", "gy"), None, None),
        ),
        out_specs=P("sec", None, "gx", "gy"),
        check_vma=False,
    )
```

```python
import jax
import jax.numpy as jnp
from jax import lax
from jax.sharding import PartitionSpec as P

PATCH = 2
PW = 128
SWEEPS = 8


OMEGA = 0.8
KAPPA = 0.5
HIGHEST = lax.Precision.HIGHEST


def shifted(block, dx, dy):
    nx = lax.axis_size("gx")
    ny = lax.axis_size("gy")
    pairs = []
    for a in range(nx):
        for b in range(ny):
            sa, sb = a + dx, b + dy
            if 0 <= sa < nx and 0 <= sb < ny:
                pairs.append((sa * ny + sb, a * ny + b))
    return lax.ppermute(block, ("gx", "gy"), pairs)


def columns(cells, start, w):
    sel = onehot(start + jnp.arange(w, dtype=jnp.int32), cells.shape[2])
    return jnp.einsum("jc,lrc->ljr", sel, cells, precision=HIGHEST)


def uncolumns(strips):
    return jnp.einsum("ljr,jm->lrm", strips, jnp.eye(strips.shape[1], dtype=strips.dtype), precision=HIGHEST)


def halo(cells, w):
    cols = cells.shape[2]
    index = jnp.concatenate([jnp.arange(cols - w, cols, dtype=jnp.int32), jnp.arange(w, dtype=jnp.int32)])
    both = jnp.einsum("jc,lrc->ljr", onehot(index, cols), cells, precision=HIGHEST)
    back = uncolumns(jnp.concatenate([shifted(both[:, :w], 0, -1), shifted(both[:, w:], 0, 1)], axis=1))
    west, east = back[:, :, :w], back[:, :, w:]
    wide = jnp.concatenate([west, cells, east], axis=2)
    north = shifted(wide[:, -w:], -1, 0)
    south = shifted(wide[:, :w], 1, 0)
    return jnp.concatenate([north, wide, south], axis=1)


def relax(field, visc, invd, force):
    padded = jnp.pad(field, ((0, 0), (1, 1), (1, 1)))
    beside = padded[:, 2:, 1:-1] + padded[:, :-2, 1:-1]
    beside = beside + padded[:, 1:-1, 2:] + padded[:, 1:-1, :-2]
    return (1.0 - OMEGA) * field + OMEGA * invd * (force + visc * beside)


def sweeps(ext, visc, invd, force, count, w):
    for _ in range(count - 1):
        ext = relax(ext, visc, invd, force)
    inner = (slice(None), slice(w, -w), slice(w, -w))
    beside = ext[:, w + 1:-w + 1, w:-w] + ext[:, w - 1:-w - 1, w:-w]
    beside = beside + ext[:, w:-w, w + 1:-w + 1] + ext[:, w:-w, w - 1:-w - 1]
    return (1.0 - OMEGA) * ext[inner] + OMEGA * invd[inner] * (force[inner] + visc[inner] * beside)


def swap_sec(x):
    return lax.ppermute(x, "sec", [(0, 1), (1, 0)])


def onehot(index, size):
    return (index[:, None] == jnp.arange(size, dtype=jnp.int32)[None, :]).astype(jnp.float32)


def pick(sel, patches):
    return jnp.einsum("jk,lkrc->jlrc", sel, patches, precision=HIGHEST)


def spread(sel, values):
    return jnp.einsum("jk,jlrc->lkrc", sel, values, precision=HIGHEST)


def selectors(source_patch, owner, cavity_map, npatch):
    groups, slots_per = cavity_map.shape[2], cavity_map.shape[3]
    nslot = groups * slots_per
    sources = source_patch[0]
    dest = owner[0, :, 0]
    count = dest.shape[0]
    earlier = jnp.arange(count)[None, :] < jnp.arange(count)[:, None]
    rank = jnp.sum((dest[:, None] == dest[None, :]) & earlier, axis=1).astype(jnp.int32)
    slot = dest * slots_per + rank
    send_sel = jnp.dot(onehot(slot, nslot).T, onehot(sources, npatch), precision=HIGHEST)
    cav_other = swap_sec(cavity_map[0, 0].reshape(-1))
    recv_sel = onehot(cav_other, npatch)
    return send_sel, recv_sel, groups, slots_per


def couple(x1, sel):
    send_sel, recv_sel, groups, slots_per = sel
    levels, rows, cols = x1.shape
    npatch = rows // PATCH
    nslot = groups * slots_per
    mine = x1.reshape(levels, npatch, PATCH, cols)
    other = swap_sec(mine)
    sent = pick(send_sel, mine)
    local = pick(recv_sel, other)
    half = slots_per * levels * PATCH
    chunk = (groups, half, cols)
    outgoing = jnp.concatenate([sent.reshape(chunk), local.reshape(chunk)], axis=1)
    incoming = lax.all_to_all(outgoing, ("gx", "gy"), 0, 0, tiled=True)
    arrived = incoming[:, :half].reshape(nslot, levels, PATCH, cols)
    answer = incoming[:, half:].reshape(nslot, levels, PATCH, cols)
    for_other = spread(recv_sel, KAPPA * arrived)
    for_mine = spread(send_sel, answer * jnp.tanh(sent))
    updated = mine + swap_sec(for_other) + for_mine
    return updated.reshape(levels, rows, cols)


def body(adjoint_state, forcing, viscosity, reaction, source_patch, owner, cavity_map):
    w = SWEEPS // 2
    levels, rows, cols = adjoint_state.shape[1:]
    invd = 1.0 / (4.0 * viscosity + reaction)
    stacked = jnp.concatenate([adjoint_state[0], forcing[0], viscosity, invd], axis=0)
    ext = halo(stacked, w)
    field = ext[:levels]
    force = ext[levels:2 * levels]
    visc = ext[2 * levels:2 * levels + 1]
    inv_wide = ext[2 * levels + 1:]
    sel = selectors(source_patch, owner, cavity_map, rows // PATCH)
    x1 = sweeps(field, visc, inv_wide, force, w, w)
    x2 = couple(x1, sel)
    out = sweeps(halo(x2, w), visc, inv_wide, force, SWEEPS - w, w)
    return out[None]


def solution(mesh):
    return jax.shard_map(
        body,
        mesh=mesh,
        in_specs=(
            P("sec", None, "gx", "gy"),
            P("sec", None, "gx", "gy"),
            P("sec", "gx", "gy"),
            P("sec", "gx", "gy"),
            P("sec", ("gx", "gy")),
            P("sec", ("gx", "gy"), None),
            P("sec", ("gx", "gy"), None, None),
        ),
        out_specs=P("sec", None, "gx", "gy"),
        check_vma=False,
    )
```

```python
import jax
import jax.numpy as jnp
from jax import lax
from jax.sharding import PartitionSpec as P

PATCH = 2
PW = 128
SWEEPS = 8


OMEGA = 0.8
KAPPA = 0.5
HIGHEST = lax.Precision.HIGHEST


def shifted(block, dx, dy):
    nx = lax.axis_size("gx")
    ny = lax.axis_size("gy")
    pairs = []
    for a in range(nx):
        for b in range(ny):
            sa, sb = a + dx, b + dy
            if 0 <= sa < nx and 0 <= sb < ny:
                pairs.append((sa * ny + sb, a * ny + b))
    return lax.ppermute(block, ("gx", "gy"), pairs)


def columns(cells, start, w):
    sel = onehot(start + jnp.arange(w, dtype=jnp.int32), cells.shape[2])
    return jnp.einsum("jc,lrc->ljr", sel, cells, precision=HIGHEST)


def uncolumns(strips):
    return jnp.einsum("ljr,jm->lrm", strips, jnp.eye(strips.shape[1], dtype=strips.dtype), precision=HIGHEST)


def halo(cells, w):
    cols = cells.shape[2]
    index = jnp.concatenate([jnp.arange(cols - w, cols, dtype=jnp.int32), jnp.arange(w, dtype=jnp.int32)])
    both = jnp.einsum("jc,lrc->ljr", onehot(index, cols), cells, precision=HIGHEST)
    west = uncolumns(shifted(both[:, :w], 0, -1))
    east = uncolumns(shifted(both[:, w:], 0, 1))
    wide = jnp.concatenate([west, cells, east], axis=2)
    north = shifted(wide[:, -w:], -1, 0)
    south = shifted(wide[:, :w], 1, 0)
    return jnp.concatenate([north, wide, south], axis=1)


def relax(field, visc, invd, force):
    padded = jnp.pad(field, ((0, 0), (1, 1), (1, 1)))
    beside = padded[:, 2:, 1:-1] + padded[:, :-2, 1:-1]
    beside = beside + padded[:, 1:-1, 2:] + padded[:, 1:-1, :-2]
    return (1.0 - OMEGA) * field + OMEGA * invd * (force + visc * beside)


def sweeps(ext, visc, invd, force, count, w):
    for _ in range(count - 1):
        ext = relax(ext, visc, invd, force)
    inner = (slice(None), slice(w, -w), slice(w, -w))
    beside = ext[:, w + 1:-w + 1, w:-w] + ext[:, w - 1:-w - 1, w:-w]
    beside = beside + ext[:, w:-w, w + 1:-w + 1] + ext[:, w:-w, w - 1:-w - 1]
    return (1.0 - OMEGA) * ext[inner] + OMEGA * invd[inner] * (force[inner] + visc[inner] * beside)


def swap_sec(x):
    return lax.ppermute(x, "sec", [(0, 1), (1, 0)])


def onehot(index, size):
    return (index[:, None] == jnp.arange(size, dtype=jnp.int32)[None, :]).astype(jnp.float32)


def pick(sel, patches):
    return jnp.einsum("jk,lkrc->jlrc", sel, patches, precision=HIGHEST)


def spread(sel, values):
    return jnp.einsum("jk,jlrc->lkrc", sel, values, precision=HIGHEST)


def selectors(source_patch, owner, cavity_map, npatch):
    groups, slots_per = cavity_map.shape[2], cavity_map.shape[3]
    nslot = groups * slots_per
    sources = source_patch[0]
    dest = owner[0, :, 0]
    count = dest.shape[0]
    earlier = jnp.arange(count)[None, :] < jnp.arange(count)[:, None]
    rank = jnp.sum((dest[:, None] == dest[None, :]) & earlier, axis=1).astype(jnp.int32)
    slot = dest * slots_per + rank
    send_sel = jnp.dot(onehot(slot, nslot).T, onehot(sources, npatch), precision=HIGHEST)
    cav_other = swap_sec(cavity_map[0, 0].reshape(-1))
    recv_sel = onehot(cav_other, npatch)
    return send_sel, recv_sel, groups, slots_per


def couple(x1, sel):
    send_sel, recv_sel, groups, slots_per = sel
    levels, rows, cols = x1.shape
    npatch = rows // PATCH
    nslot = groups * slots_per
    mine = x1.reshape(levels, npatch, PATCH, cols)
    other = swap_sec(mine)
    sent = pick(send_sel, mine)
    local = pick(recv_sel, other)
    half = slots_per * levels * PATCH
    chunk = (groups, half, cols)
    outgoing = jnp.stack([sent.reshape(chunk), local.reshape(chunk)], axis=1)
    incoming = lax.all_to_all(outgoing, ("gx", "gy"), 0, 0, tiled=True)
    arrived = incoming[:, 0].reshape(nslot, levels, PATCH, cols)
    answer = incoming[:, 1].reshape(nslot, levels, PATCH, cols)
    for_other = spread(recv_sel, KAPPA * arrived)
    for_mine = spread(send_sel, answer * jnp.tanh(sent))
    updated = mine + swap_sec(for_other) + for_mine
    return updated.reshape(levels, rows, cols)


def body(adjoint_state, forcing, viscosity, reaction, source_patch, owner, cavity_map):
    w = SWEEPS // 2
    levels, rows, cols = adjoint_state.shape[1:]
    invd = 1.0 / (4.0 * viscosity + reaction)
    stacked = jnp.concatenate([adjoint_state[0], forcing[0], viscosity, invd], axis=0)
    ext = halo(stacked, w)
    field = ext[:levels]
    force = ext[levels:2 * levels]
    visc = ext[2 * levels:2 * levels + 1]
    inv_wide = ext[2 * levels + 1:]
    sel = selectors(source_patch, owner, cavity_map, rows // PATCH)
    x1 = sweeps(field, visc, inv_wide, force, w, w)
    x2 = couple(x1, sel)
    out = sweeps(halo(x2, w), visc, inv_wide, force, SWEEPS - w, w)
    return out[None]


def solution(mesh):
    return jax.shard_map(
        body,
        mesh=mesh,
        in_specs=(
            P("sec", None, "gx", "gy"),
            P("sec", None, "gx", "gy"),
            P("sec", "gx", "gy"),
            P("sec", "gx", "gy"),
            P("sec", ("gx", "gy")),
            P("sec", ("gx", "gy"), None),
            P("sec", ("gx", "gy"), None, None),
        ),
        out_specs=P("sec", None, "gx", "gy"),
        check_vma=False,
    )
```
